256 devices in a mesh: req: 64 (over z, y_lo, x), tp: 4 (over y_hi, core).
Axes of the slice: x: 4, y: 4 (y_hi: 2, y_lo: 2; y = y_hi * 2 + y_lo), z: 8, core: 2. Of those that a mesh axis runs over, the one named last changes fastest.
Arguments:
- hidden: bfloat16 [32768, 4096], P(('req', 'tp')), may hold values from -6 to 6
- norm_gain: bfloat16 [4096], replicated, may hold values from 0.099609375 to 1.8984375
- w_qkv: bfloat16 [4096, 3072], P('req', 'tp'), may hold values from -0.09375 to 0.09375
- w_out: bfloat16 [2048, 4096], P('tp', 'req'), may hold values from -0.125 to 0.125
- lengths: int32 [256], replicated, may hold values from 1 to 3072, as said below
- deal: int32 [256], replicated, may hold values from 0 to 255, as said below
- pages: int32 [256, 24], P('req'), may hold values from 0 to 95, as said below
- pool: bfloat16 [6144, 128, 1024], P('req', None, 'tp'), may hold values from -360 to 360
Outputs:
- attn_out: bfloat16 [32768, 4096], P(('req', 'tp'))
- new_kv: bfloat16 [32768, 1024], P('req', 'tp')
The draws below stay inside these ranges and needn't reach their ends.
Inputs may be any that keep to these rules, and one draw needn't show every extreme that they name: `lengths`: at least one request has exactly 3072 cached tokens. `deal`: a permutation of the requests. `pages`: the 4 rows of one req index together hold each page number of its pool block once.
All inputs are finite; a program needn't handle non-finite values.
Results may differ from the reference program's by a relative error of at most 0.01.
The reference program's roundings to bfloat16 on the way count: a program that leaves them out, or rounds other values in their place, can miss the bound.
Values may be sent and summed in bfloat16 or wider, within the bound.
No kernel may reach another device: no remote copies, remote signals or barrier semaphores. Data moves between devices by JAX's collectives and lax.ppermute only.
A program may use at most 128 MiB of HBM per device.

```python
import math
import jax
import jax.numpy as jnp
from jax import lax

D = 4096
HEAD = 128
QH = 16
KVH = 4
PAGE = 128
MAXP = 24
R_DEV = 4
NEW = 128
REQS = 256
TOKENS = 32768
POOL = 6144
N_TP = 4


def deal_parts(key):
    base_key = jax.random.fold_in(key, 11)
    length_key, spot_key, order_key = jax.random.split(base_key, 3)
    longest = MAXP * PAGE
    drawn_lengths = jax.random.randint(length_key, (REQS,), 1, longest + 1)
    chosen = jax.random.randint(spot_key, (), 0, REQS)
    drawn_lengths = drawn_lengths.at[chosen].set(longest)
    tiebreak = jax.random.permutation(order_key, REQS)
    ranking = drawn_lengths * REQS + tiebreak
    ordered = jnp.argsort(-ranking, stable=True).astype(jnp.int32)
    ranks = jnp.arange(REQS, dtype=jnp.int32)
    holders = REQS // R_DEV
    round_number = ranks // holders
    within = ranks % holders
    holder = jnp.where(round_number % 2 == 0, within, holders - 1 - within)
    slot_index = holder * R_DEV + round_number
    dealt = jnp.zeros((REQS,), jnp.int32).at[slot_index].set(ordered)
    return (drawn_lengths.astype(jnp.int32), dealt)


def draw_lengths(key, part):
    return deal_parts(key)[0]


def draw_deal(key, part):
    return deal_parts(key)[1]


def draw_pages(key, part):
    holders = REQS // R_DEV
    subkeys = jax.random.split(jax.random.fold_in(key, 23), holders)

    def shuffle(subkey):
        return jax.random.permutation(subkey, R_DEV * MAXP)
    table = jax.vmap(shuffle)(subkeys)
    return table.reshape(REQS, MAXP).astype(jnp.int32)


def draw_pool(key, part):
    normal_key = jax.random.fold_in(key, 31)
    base_values = jnp.clip(jax.random.normal(normal_key, (POOL, PAGE, KVH, 2, HEAD), jnp.float32), -6.0, 6.0) * 1.5
    return base_values.reshape(POOL, PAGE, KVH * 2 * HEAD).astype(jnp.bfloat16)


def steps_of(own_key, shape, shards, least, largest):
    def one(axis_at, shards_of):
        heights = jax.random.uniform(jax.random.fold_in(jax.random.fold_in(own_key, 6), axis_at), (shards_of,), jnp.float32, least / len(shards), largest / len(shards))
        return jnp.repeat(jnp.exp(heights), shape[axis_at] // shards_of).reshape((-1,) + (1,) * (len(shape) - axis_at - 1))

    level = one(*shards[0])
    for cut in shards[1:]:
        level = level * one(*cut)
    return level


def gaussian(own_key, dims, scale, reach, shards=(), kind=jnp.bfloat16):
    array = scale * jax.random.normal(own_key, dims, jnp.float32)
    if shards:
        array = array * steps_of(own_key, dims, shards, -0.22, 0.18)
    return jnp.clip(array, -reach, reach).astype(kind)


def setup_inputs(seed: int = 0) -> dict:
    streams_of = jax.random.split(jax.random.key(seed), 9)
    return {
        "hidden": gaussian(streams_of[0], (TOKENS, D), 1.0, 6.0, ((0, 256),)),
        "norm_gain": jnp.clip(1.0 + 0.18 * jax.random.normal(streams_of[1], (D,), jnp.float32), 0.099609375, 1.8984375).astype(jnp.bfloat16),
        "w_qkv": gaussian(streams_of[2], (D, KVH * (QH // KVH + 2) * HEAD), D ** -0.5, 0.09375, ((0, 64), (1, 4))),
        "w_out": gaussian(streams_of[3], (QH * HEAD, D), (QH * HEAD) ** -0.5, 0.125, ((0, 4), (1, 64))),
        "lengths": draw_lengths(jax.random.fold_in(streams_of[8], 71), 0),
        "deal": draw_deal(jax.random.fold_in(streams_of[8], 71), 0),
        "pages": draw_pages(jax.random.fold_in(streams_of[8], 71), 0),
        "pool": draw_pool(jax.random.fold_in(streams_of[8], 71), 0),
    }


def rotate(values, position):
    half = values.shape[-1] // 2
    freqs = 500000.0 ** (-(jnp.arange(half, dtype=jnp.float32) * 2.0 / values.shape[-1]))
    angles = position.astype(jnp.float32)[:, None] * freqs[None, :]
    target = (angles.shape[0],) + (1,) * (values.ndim - 2) + (half,)
    cosine = jnp.cos(angles).reshape(target)
    sine = jnp.sin(angles).reshape(target)
    former = values[..., :half]
    latter = values[..., half:]
    return jnp.concatenate([former * cosine - latter * sine, latter * cosine + former * sine], -1)

def reference(hidden, norm_gain, w_qkv, w_out, lengths, deal, pages, pool):
    states = hidden.astype(jnp.float32)
    mean_square = lax.optimization_barrier(jnp.mean(states * states, axis=1, keepdims=True))
    normed = (states * lax.rsqrt(mean_square + 1e-05) * norm_gain.astype(jnp.float32)).astype(jnp.bfloat16)
    projected = jnp.dot(normed, w_qkv, preferred_element_type=jnp.float32).astype(jnp.bfloat16)
    group = QH // KVH
    projected = projected.reshape(TOKENS, KVH, group + 2, HEAD)
    slot_length = lengths[deal]
    position = jnp.repeat(slot_length, NEW) + jnp.tile(jnp.arange(NEW, dtype=jnp.int32), REQS)
    queries = rotate(projected[:, :, :group].astype(jnp.float32), position).astype(jnp.bfloat16)
    keys_new = rotate(projected[:, :, group].astype(jnp.float32), position).astype(jnp.bfloat16)
    values_new = projected[:, :, group + 1]
    new_kv = jnp.stack([keys_new, values_new], 2).reshape(TOKENS, KVH * 2 * HEAD)
    pool_view = pool.reshape(POOL, PAGE, KVH, 2, HEAD)
    score_scale = 1.0 / math.sqrt(HEAD)
    cached_span = MAXP * PAGE

    def one_slot(slot_number):
        begin = slot_number * NEW
        query_matrix = lax.dynamic_slice_in_dim(queries, begin, NEW, 0).astype(jnp.float32)
        recent_key_rows = lax.dynamic_slice_in_dim(keys_new, begin, NEW, 0).astype(jnp.float32)
        recent_value_rows = lax.dynamic_slice_in_dim(values_new, begin, NEW, 0).astype(jnp.float32)
        page_rows = slot_number // R_DEV * (R_DEV * MAXP) + pages[slot_number]
        cache = pool_view[page_rows].reshape(cached_span, KVH, 2, HEAD).astype(jnp.float32)
        length = slot_length[slot_number]
        cached_scores = jnp.einsum('nhgd,khd->hgnk', query_matrix, cache[:, :, 0]) * score_scale
        cached_scores = jnp.where(jnp.arange(cached_span, dtype=jnp.int32) < length, cached_scores, -jnp.inf)
        recent_score_rows = jnp.einsum('eksv,qkv->kseq', query_matrix, recent_key_rows) * score_scale
        causal = jnp.arange(NEW)[:, None] >= jnp.arange(NEW)[None, :]
        recent_score_rows = jnp.where(causal, recent_score_rows, -jnp.inf)
        row_max = jnp.maximum(cached_scores.max(-1), recent_score_rows.max(-1))[..., None]
        cached_exp = jnp.exp(cached_scores - row_max)
        recent_exponent = jnp.exp(recent_score_rows - row_max)
        total = cached_exp.sum(-1) + recent_exponent.sum(-1)
        cached_weights = lax.optimization_barrier(cached_exp.astype(jnp.bfloat16)).astype(jnp.float32)
        recent_weight_rows = lax.optimization_barrier(recent_exponent.astype(jnp.bfloat16)).astype(jnp.float32)
        summed_total = jnp.einsum('hgnk,khd->hgnd', cached_weights, cache[:, :, 1])
        summed_total = summed_total + jnp.einsum('tvqa,ats->tvqs', recent_weight_rows, recent_value_rows)
        context = (summed_total / total[..., None]).astype(jnp.bfloat16)
        return context.transpose(2, 0, 1, 3).reshape(NEW, QH * HEAD)
    contexts = lax.map(one_slot, jnp.arange(REQS, dtype=jnp.int32))
    context = contexts.reshape(TOKENS, QH * HEAD)
    width = QH * HEAD // N_TP
    attn = jnp.zeros((TOKENS, D), jnp.float32)
    for group_number in range(N_TP):
        partial_sum = jnp.dot(context[:, group_number * width:(group_number + 1) * width], w_out[group_number * width:(group_number + 1) * width], preferred_element_type=jnp.float32)
        attn = attn + lax.optimization_barrier(partial_sum.astype(jnp.bfloat16)).astype(jnp.float32)
    return (attn.astype(jnp.bfloat16), new_kv)
```

```python
import math

import jax
import jax.numpy as jnp
from jax import lax
from jax.sharding import PartitionSpec as P

HEAD = 128
QH = 16
KVH = 4
PAGE = 128
NEW = 128


def rotate(values, position):
    half = values.shape[-1] // 2
    freqs = 500000.0 ** (-(jnp.arange(half, dtype=jnp.float32) * 2.0 / values.shape[-1]))
    angles = position.astype(jnp.float32)[:, None] * freqs[None, :]
    target = (angles.shape[0],) + (1,) * (values.ndim - 2) + (half,)
    cosine = jnp.cos(angles).reshape(target)
    sine = jnp.sin(angles).reshape(target)
    former = values[..., :half]
    latter = values[..., half:]
    return jnp.concatenate([former * cosine - latter * sine, latter * cosine + former * sine], -1)


def fresh_scores_of(query_matrix, recent_key_rows, score_scale):
    scores = (
        jnp.einsum(
            "eksv,qkv->kseq", query_matrix, recent_key_rows, preferred_element_type=jnp.float32
        )
        * score_scale
    )
    count_new = query_matrix.shape[0]
    causal = jnp.arange(count_new)[:, None] >= jnp.arange(count_new)[None, :]
    return jnp.where(causal, scores, -jnp.inf)


def value_weighted_rows(weights, values, form):
    return jnp.einsum(
        form, weights.astype(jnp.bfloat16), values, preferred_element_type=jnp.float32
    )


def padded_attention(
    query_matrix, recent_key_rows, recent_value_rows, pool_view, page_row, length, score_scale
):
    heads_here = pool_view.shape[2]
    cache = pool_view[page_row].reshape(-1, heads_here, 2, HEAD)
    span = cache.shape[0]
    cached_scores = (
        jnp.einsum(
            "nhgd,khd->hgnk", query_matrix, cache[:, :, 0], preferred_element_type=jnp.float32
        )
        * score_scale
    )
    cached_scores = jnp.where(jnp.arange(span, dtype=jnp.int32) < length, cached_scores, -jnp.inf)
    recent_score_rows = fresh_scores_of(query_matrix, recent_key_rows, score_scale)
    row_max = jnp.maximum(cached_scores.max(-1), recent_score_rows.max(-1))[..., None]
    cached_exp = jnp.exp(cached_scores - row_max)
    recent_exponent = jnp.exp(recent_score_rows - row_max)
    total = cached_exp.sum(-1) + recent_exponent.sum(-1)
    summed_total = value_weighted_rows(cached_exp, cache[:, :, 1], "hgnk,khd->hgnd")
    summed_total = summed_total + value_weighted_rows(
        recent_exponent, recent_value_rows, "tvqa,ats->tvqs"
    )
    return summed_total / total[..., None]


REQ_AXES = ("z", "ylo", "x")
TP_AXES = ("yhi", "core")


def staged_gather(values, axes, axis):
    for name in reversed(axes):
        values = lax.all_gather(values, name, axis=axis, tiled=True)
    return values


def per_device(hidden, norm_gain, w_qkv, w_out, lengths, deal, pages, pool):
    states = hidden.astype(jnp.float32)
    mean_square = jnp.mean(states * states, axis=1, keepdims=True)
    normed = (states * lax.rsqrt(mean_square + 1e-05) * norm_gain.astype(jnp.float32)).astype(
        jnp.bfloat16
    )
    gathered = lax.all_gather(normed, TP_AXES, axis=0, tiled=True)
    tok_rows = gathered.shape[0]
    projected = jnp.dot(
        gathered,
        staged_gather(w_qkv, REQ_AXES, 0),
        preferred_element_type=jnp.float32,
    ).astype(jnp.bfloat16)
    full_out = staged_gather(w_out, REQ_AXES, 1)
    group = QH // KVH
    heads_here = w_qkv.shape[1] // ((group + 2) * HEAD)
    slot_count = tok_rows // NEW
    slot_ids = lax.axis_index(REQ_AXES) * slot_count + jnp.arange(slot_count, dtype=jnp.int32)
    slot_length = lengths[deal[slot_ids]]
    position = jnp.repeat(slot_length, NEW) + jnp.tile(jnp.arange(NEW, dtype=jnp.int32), slot_count)
    projected = projected.reshape(tok_rows, heads_here, group + 2, HEAD)
    queries = rotate(projected[:, :, :group].astype(jnp.float32), position).astype(jnp.bfloat16)
    keys_new = rotate(projected[:, :, group].astype(jnp.float32), position).astype(jnp.bfloat16)
    values_new = projected[:, :, group + 1]
    new_kv = jnp.stack([keys_new, values_new], 2).reshape(tok_rows, heads_here * 2 * HEAD)
    pool_view = pool.reshape(pool.shape[0], PAGE, heads_here, 2, HEAD)
    score_scale = 1.0 / math.sqrt(HEAD)

    def attend(local_slot):
        begin = local_slot * NEW
        query_matrix = lax.dynamic_slice_in_dim(queries, begin, NEW, 0)
        recent_key_rows = lax.dynamic_slice_in_dim(keys_new, begin, NEW, 0)
        recent_value_rows = lax.dynamic_slice_in_dim(values_new, begin, NEW, 0)
        page_row = pages[local_slot]
        length = slot_length[local_slot]
        result = padded_attention(
            query_matrix,
            recent_key_rows,
            recent_value_rows,
            pool_view,
            page_row,
            length,
            score_scale,
        )
        result = result.astype(jnp.bfloat16)
        return result.transpose(2, 0, 1, 3).reshape(NEW, heads_here * group * HEAD)

    contexts = lax.map(attend, jnp.arange(slot_count, dtype=jnp.int32))
    context = contexts.reshape(tok_rows, heads_here * group * HEAD)
    attn_out = lax.psum_scatter(
        jnp.dot(context, full_out, preferred_element_type=jnp.float32).astype(jnp.bfloat16),
        TP_AXES,
        scatter_dimension=0,
        tiled=True,
    )
    return (attn_out, new_kv)


def solution(mesh):
    fine = jax.sharding.Mesh(mesh.devices.reshape(8, 2, 4, 2, 2), REQ_AXES + TP_AXES)
    in_specs = (
        P(REQ_AXES + TP_AXES, None),
        P(),
        P(REQ_AXES, TP_AXES),
        P(TP_AXES, REQ_AXES),
        P(),
        P(),
        P(REQ_AXES, None),
        P(REQ_AXES, None, TP_AXES),
    )
    out_specs = (P(REQ_AXES + TP_AXES, None), P(REQ_AXES, TP_AXES))
    return jax.shard_map(
        per_device, mesh=fine, in_specs=in_specs, out_specs=out_specs, check_vma=False
    )
```

```python
import math

import jax
import jax.numpy as jnp
from jax import lax
from jax.sharding import PartitionSpec as P

HEAD = 128
QH = 16
KVH = 4
PAGE = 128
NEW = 128


def rotate(values, position):
    half = values.shape[-1] // 2
    freqs = 500000.0 ** (-(jnp.arange(half, dtype=jnp.float32) * 2.0 / values.shape[-1]))
    angles = position.astype(jnp.float32)[:, None] * freqs[None, :]
    target = (angles.shape[0],) + (1,) * (values.ndim - 2) + (half,)
    cosine = jnp.cos(angles).reshape(target)
    sine = jnp.sin(angles).reshape(target)
    former = values[..., :half]
    latter = values[..., half:]
    return jnp.concatenate([former * cosine - latter * sine, latter * cosine + former * sine], -1)


def fresh_scores_of(query_matrix, recent_key_rows, score_scale):
    scores = (
        jnp.einsum("esv,qv->seq", query_matrix, recent_key_rows, preferred_element_type=jnp.float32)
        * score_scale
    )
    count_new = query_matrix.shape[0]
    causal = jnp.arange(count_new)[:, None] >= jnp.arange(count_new)[None, :]
    return jnp.where(causal, scores, -jnp.inf)


def value_weighted_rows(weights, values, form):
    return jnp.einsum(
        form, weights.astype(jnp.bfloat16), values, preferred_element_type=jnp.float32
    )


def padded_attention(
    query_matrix, recent_key_rows, recent_value_rows, pool, page_row, length, score_scale
):
    cache = pool[page_row].reshape(-1, 2 * HEAD)
    span = cache.shape[0]
    cached_scores = (
        jnp.einsum("ngd,kd->gnk", query_matrix, cache[:, :HEAD], preferred_element_type=jnp.float32)
        * score_scale
    )
    cached_scores = jnp.where(jnp.arange(span, dtype=jnp.int32) < length, cached_scores, -jnp.inf)
    recent_score_rows = fresh_scores_of(query_matrix, recent_key_rows, score_scale)
    row_max = jnp.maximum(cached_scores.max(-1), recent_score_rows.max(-1))[..., None]
    cached_exp = jnp.exp(cached_scores - row_max)
    recent_exponent = jnp.exp(recent_score_rows - row_max)
    total = cached_exp.sum(-1) + recent_exponent.sum(-1)
    summed_total = value_weighted_rows(cached_exp, cache[:, HEAD:], "gnk,kd->gnd")
    summed_total = summed_total + value_weighted_rows(
        recent_exponent, recent_value_rows, "vqa,as->vqs"
    )
    return summed_total / total[..., None]


REQ_AXES = ("z", "ylo", "x")
TP_AXES = ("yhi", "core")


def staged_gather(values, axes, axis):
    for name in reversed(axes):
        values = lax.all_gather(values, name, axis=axis, tiled=True)
    return values


def per_device(hidden, norm_gain, w_qkv, w_out, lengths, deal, pages, pool):
    states = hidden.astype(jnp.float32)
    mean_square = jnp.mean(states * states, axis=1, keepdims=True)
    normed = (states * lax.rsqrt(mean_square + 1e-05) * norm_gain.astype(jnp.float32)).astype(
        jnp.bfloat16
    )
    gathered = lax.all_gather(lax.all_gather(normed, "core", axis=0, tiled=True), "yhi", axis=0, tiled=True)
    tok_rows = gathered.shape[0]
    projected = jnp.dot(
        gathered,
        staged_gather(w_qkv, REQ_AXES, 0),
        preferred_element_type=jnp.float32,
    ).astype(jnp.bfloat16)
    full_out = staged_gather(w_out, REQ_AXES, 1)
    group = QH // KVH
    heads_here = w_qkv.shape[1] // ((group + 2) * HEAD)
    assert heads_here == 1 and pool.shape[2] == 2 * HEAD
    slot_count = tok_rows // NEW
    slot_ids = lax.axis_index(REQ_AXES) * slot_count + jnp.arange(slot_count, dtype=jnp.int32)
    slot_length = lengths[deal[slot_ids]]
    position = jnp.repeat(slot_length, NEW) + jnp.tile(jnp.arange(NEW, dtype=jnp.int32), slot_count)
    projected = projected.reshape(tok_rows, group + 2, HEAD)
    queries = rotate(projected[:, :group].astype(jnp.float32), position).astype(jnp.bfloat16)
    keys_new = rotate(projected[:, group].astype(jnp.float32), position).astype(jnp.bfloat16)
    values_new = projected[:, group + 1]
    new_kv = jnp.concatenate([keys_new, values_new], 1)
    score_scale = 1.0 / math.sqrt(HEAD)

    def attend(local_slot):
        begin = local_slot * NEW
        query_matrix = lax.dynamic_slice_in_dim(queries, begin, NEW, 0)
        recent_key_rows = lax.dynamic_slice_in_dim(keys_new, begin, NEW, 0)
        recent_value_rows = lax.dynamic_slice_in_dim(values_new, begin, NEW, 0)
        page_row = pages[local_slot]
        length = slot_length[local_slot]
        result = padded_attention(
            query_matrix,
            recent_key_rows,
            recent_value_rows,
            pool,
            page_row,
            length,
            score_scale,
        )
        result = result.astype(jnp.bfloat16)
        return result.transpose(1, 0, 2).reshape(NEW, group * HEAD)

    n_hi = lax.axis_size("yhi")
    n_core = lax.axis_size("core")
    order = jnp.arange(slot_count, dtype=jnp.int32)
    order = (order % n_hi) * n_core + order // n_hi
    contexts = lax.map(attend, order)
    context = contexts.reshape(tok_rows, group * HEAD)
    partial = jnp.dot(context, full_out, preferred_element_type=jnp.float32).astype(jnp.bfloat16)
    partial = lax.psum_scatter(partial, "core", scatter_dimension=0, tiled=True)
    attn_out = lax.psum_scatter(partial, "yhi", scatter_dimension=0, tiled=True)
    return (attn_out, new_kv)


def solution(mesh):
    fine = jax.sharding.Mesh(mesh.devices.reshape(8, 2, 4, 2, 2), REQ_AXES + TP_AXES)
    in_specs = (
        P(REQ_AXES + TP_AXES, None),
        P(),
        P(REQ_AXES, TP_AXES),
        P(TP_AXES, REQ_AXES),
        P(),
        P(),
        P(REQ_AXES, None),
        P(REQ_AXES, None, TP_AXES),
    )
    out_specs = (P(REQ_AXES + TP_AXES, None), P(REQ_AXES, TP_AXES))
    return jax.shard_map(
        per_device, mesh=fine, in_specs=in_specs, out_specs=out_specs, check_vma=False
    )
```

```python
import math

import jax
import jax.numpy as jnp
from jax import lax
from jax.sharding import PartitionSpec as P

HEAD = 128
QH = 16
KVH = 4
PAGE = 128
NEW = 128


def rotate(values, position):
    half = values.shape[-1] // 2
    freqs = 500000.0 ** (-(jnp.arange(half, dtype=jnp.float32) * 2.0 / values.shape[-1]))
    angles = position.astype(jnp.float32)[:, None] * freqs[None, :]
    target = (angles.shape[0],) + (1,) * (values.ndim - 2) + (half,)
    cosine = jnp.cos(angles).reshape(target)
    sine = jnp.sin(angles).reshape(target)
    former = values[..., :half]
    latter = values[..., half:]
    return jnp.concatenate([former * cosine - latter * sine, latter * cosine + former * sine], -1)


def fresh_scores_of(query_matrix, recent_key_rows, score_scale):
    scores = (
        jnp.einsum("esv,qv->seq", query_matrix, recent_key_rows, preferred_element_type=jnp.float32)
        * score_scale
    )
    count_new = query_matrix.shape[0]
    causal = jnp.arange(count_new)[:, None] >= jnp.arange(count_new)[None, :]
    return jnp.where(causal, scores, -jnp.inf)


def value_weighted_rows(weights, values, form):
    return jnp.einsum(
        form, weights.astype(jnp.bfloat16), values, preferred_element_type=jnp.float32
    )


def padded_attention(
    query_matrix, recent_key_rows, recent_value_rows, pool, page_row, length, score_scale
):
    cache = pool[page_row].reshape(-1, 2 * HEAD)
    span = cache.shape[0]
    cached_scores = (
        jnp.einsum("ngd,kd->gnk", query_matrix, cache[:, :HEAD], preferred_element_type=jnp.float32)
        * score_scale
    )
    cached_scores = jnp.where(jnp.arange(span, dtype=jnp.int32) < length, cached_scores, -jnp.inf)
    recent_score_rows = fresh_scores_of(query_matrix, recent_key_rows, score_scale)
    row_max = jnp.maximum(cached_scores.max(-1), recent_score_rows.max(-1))[..., None]
    cached_exp = jnp.exp(cached_scores - row_max)
    recent_exponent = jnp.exp(recent_score_rows - row_max)
    total = cached_exp.sum(-1) + recent_exponent.sum(-1)
    summed_total = value_weighted_rows(cached_exp, cache[:, HEAD:], "gnk,kd->gnd")
    summed_total = summed_total + value_weighted_rows(
        recent_exponent, recent_value_rows, "vqa,as->vqs"
    )
    return summed_total / total[..., None]


REQ_AXES = ("z", "ylo", "x")
TP_AXES = ("yhi", "core")


def staged_gather(values, axes, axis):
    for name in reversed(axes):
        values = lax.all_gather(values, name, axis=axis, tiled=True)
    return values


def per_device(hidden, norm_gain, w_qkv, w_out, lengths, deal, pages, pool):
    states = hidden.astype(jnp.float32)
    mean_square = jnp.mean(states * states, axis=1, keepdims=True)
    normed = (states * lax.rsqrt(mean_square + 1e-05) * norm_gain.astype(jnp.float32)).astype(
        jnp.bfloat16
    )
    n_tp = lax.axis_size(TP_AXES)
    me = lax.axis_index(TP_AXES)
    arrived = [normed] + [
        lax.ppermute(normed, TP_AXES, perm=[(s, (s - k) % n_tp) for s in range(n_tp)])
        for k in range(1, n_tp)
    ]
    gathered = jnp.concatenate(arrived, 0)
    tok_rows = gathered.shape[0]
    projected = jnp.dot(
        gathered,
        staged_gather(w_qkv, REQ_AXES, 0),
        preferred_element_type=jnp.float32,
    ).astype(jnp.bfloat16)
    full_out = staged_gather(w_out, REQ_AXES, 1)
    group = QH // KVH
    heads_here = w_qkv.shape[1] // ((group + 2) * HEAD)
    assert heads_here == 1 and pool.shape[2] == 2 * HEAD
    slot_count = tok_rows // NEW
    step_slot = (me + jnp.arange(slot_count, dtype=jnp.int32)) % slot_count
    slot_ids = lax.axis_index(REQ_AXES) * slot_count + step_slot
    slot_length = lengths[deal[slot_ids]]
    position = jnp.repeat(slot_length, NEW) + jnp.tile(jnp.arange(NEW, dtype=jnp.int32), slot_count)
    projected = projected.reshape(tok_rows, group + 2, HEAD)
    queries = rotate(projected[:, :group].astype(jnp.float32), position).astype(jnp.bfloat16)
    keys_new = rotate(projected[:, group].astype(jnp.float32), position).astype(jnp.bfloat16)
    values_new = projected[:, group + 1]
    stepped_kv = jnp.concatenate([keys_new, values_new], 1)
    doubled = jnp.concatenate([stepped_kv, stepped_kv], 0)
    new_kv = lax.dynamic_slice_in_dim(doubled, ((slot_count - me) % slot_count) * NEW, tok_rows, 0)
    score_scale = 1.0 / math.sqrt(HEAD)

    total = None
    for k in range(slot_count):
        rows = slice(k * NEW, (k + 1) * NEW)
        result = padded_attention(
            queries[rows],
            keys_new[rows],
            values_new[rows],
            pool,
            pages[step_slot[k]],
            slot_length[k],
            score_scale,
        )
        context = result.astype(jnp.bfloat16).transpose(1, 0, 2).reshape(NEW, group * HEAD)
        partial = jnp.dot(context, full_out, preferred_element_type=jnp.float32).astype(
            jnp.bfloat16
        )
        if k:
            partial = lax.ppermute(partial, TP_AXES, perm=[(s, (s + k) % n_tp) for s in range(n_tp)])
        total = partial.astype(jnp.float32) if total is None else total + partial.astype(jnp.float32)
    return (total.astype(jnp.bfloat16), new_kv)


def solution(mesh):
    fine = jax.sharding.Mesh(mesh.devices.reshape(8, 2, 4, 2, 2), REQ_AXES + TP_AXES)
    in_specs = (
        P(REQ_AXES + TP_AXES, None),
        P(),
        P(REQ_AXES, TP_AXES),
        P(TP_AXES, REQ_AXES),
        P(),
        P(),
        P(REQ_AXES, None),
        P(REQ_AXES, None, TP_AXES),
    )
    out_specs = (P(REQ_AXES + TP_AXES, None), P(REQ_AXES, TP_AXES))
    return jax.shard_map(
        per_device, mesh=fine, in_specs=in_specs, out_specs=out_specs, check_vma=False
    )
```

```python
import math

import jax
import jax.numpy as jnp
from jax import lax
from jax.sharding import PartitionSpec as P

HEAD = 128
QH = 16
KVH = 4
PAGE = 128
NEW = 128


def rotate(values, position):
    half = values.shape[-1] // 2
    freqs = 500000.0 ** (-(jnp.arange(half, dtype=jnp.float32) * 2.0 / values.shape[-1]))
    angles = position.astype(jnp.float32)[:, None] * freqs[None, :]
    target = (angles.shape[0],) + (1,) * (values.ndim - 2) + (half,)
    cosine = jnp.cos(angles).reshape(target)
    sine = jnp.sin(angles).reshape(target)
    former = values[..., :half]
    latter = values[..., half:]
    return jnp.concatenate([former * cosine - latter * sine, latter * cosine + former * sine], -1)


def fresh_scores_of(query_matrix, recent_key_rows, score_scale):
    scores = (
        jnp.einsum("esv,qv->seq", query_matrix, recent_key_rows, preferred_element_type=jnp.float32)
        * score_scale
    )
    count_new = query_matrix.shape[0]
    causal = jnp.arange(count_new)[:, None] >= jnp.arange(count_new)[None, :]
    return jnp.where(causal, scores, -jnp.inf)


def value_weighted_rows(weights, values, form):
    return jnp.einsum(
        form, weights.astype(jnp.bfloat16), values, preferred_element_type=jnp.float32
    )


def padded_attention(
    query_matrix, recent_key_rows, recent_value_rows, pool, page_row, length, score_scale
):
    cache = pool[page_row].reshape(-1, 2 * HEAD)
    span = cache.shape[0]
    cached_scores = (
        jnp.einsum("ngd,kd->gnk", query_matrix, cache[:, :HEAD], preferred_element_type=jnp.float32)
        * score_scale
    )
    cached_scores = jnp.where(jnp.arange(span, dtype=jnp.int32) < length, cached_scores, -jnp.inf)
    recent_score_rows = fresh_scores_of(query_matrix, recent_key_rows, score_scale)
    row_max = jnp.maximum(cached_scores.max(-1), recent_score_rows.max(-1))[..., None]
    cached_exp = jnp.exp(cached_scores - row_max)
    recent_exponent = jnp.exp(recent_score_rows - row_max)
    total = cached_exp.sum(-1) + recent_exponent.sum(-1)
    summed_total = value_weighted_rows(cached_exp, cache[:, HEAD:], "gnk,kd->gnd")
    summed_total = summed_total + value_weighted_rows(
        recent_exponent, recent_value_rows, "vqa,as->vqs"
    )
    return summed_total / total[..., None]


REQ_AXES = ("z", "ylo", "x")
TP_AXES = ("yhi", "core")


def staged_gather(values, axes, axis):
    for name in reversed(axes):
        values = lax.all_gather(values, name, axis=axis, tiled=True)
    return values


def per_device(hidden, norm_gain, w_qkv, w_out, lengths, deal, pages, pool):
    states = hidden.astype(jnp.float32)
    mean_square = jnp.mean(states * states, axis=1, keepdims=True)
    normed = (states * lax.rsqrt(mean_square + 1e-05) * norm_gain.astype(jnp.float32)).astype(
        jnp.bfloat16
    )
    n_tp = lax.axis_size(TP_AXES)
    me = lax.axis_index(TP_AXES)
    arrived = [normed] + [
        lax.ppermute(normed, TP_AXES, perm=[(s, (s - k) % n_tp) for s in range(n_tp)])
        for k in range(1, n_tp)
    ]
    gathered = jnp.concatenate(arrived, 0)
    tok_rows = gathered.shape[0]
    projected = jnp.dot(
        gathered,
        staged_gather(w_qkv, REQ_AXES, 0),
        preferred_element_type=jnp.float32,
    ).astype(jnp.bfloat16)
    full_out = staged_gather(w_out, REQ_AXES, 1)
    group = QH // KVH
    heads_here = w_qkv.shape[1] // ((group + 2) * HEAD)
    assert heads_here == 1 and pool.shape[2] == 2 * HEAD
    slot_count = tok_rows // NEW
    step_slot = (me + jnp.arange(slot_count, dtype=jnp.int32)) % slot_count
    slot_ids = lax.axis_index(REQ_AXES) * slot_count + step_slot
    slot_length = lengths[deal[slot_ids]]
    position = jnp.repeat(slot_length, NEW) + jnp.tile(jnp.arange(NEW, dtype=jnp.int32), slot_count)
    projected = projected.reshape(tok_rows, group + 2, HEAD)
    queries = rotate(projected[:, :group].astype(jnp.float32), position).astype(jnp.bfloat16)
    keys_new = rotate(projected[:, group].astype(jnp.float32), position).astype(jnp.bfloat16)
    values_new = projected[:, group + 1]
    stepped_kv = jnp.concatenate([keys_new, values_new], 1)
    doubled = jnp.concatenate([stepped_kv, stepped_kv], 0)
    new_kv = lax.dynamic_slice_in_dim(doubled, ((slot_count - me) % slot_count) * NEW, tok_rows, 0)
    score_scale = 1.0 / math.sqrt(HEAD)

    arrived_parts = []
    pending = None
    for k in list(range(1, slot_count)) + [0]:
        rows = slice(k * NEW, (k + 1) * NEW)
        query_rows = queries[rows]
        if pending is not None:
            query_rows, made = lax.optimization_barrier((query_rows, pending[1]))
            sent_to = [(s, (s + pending[0]) % n_tp) for s in range(n_tp)]
            arrived_parts.append(lax.ppermute(made, TP_AXES, perm=sent_to))
        result = padded_attention(
            query_rows,
            keys_new[rows],
            values_new[rows],
            pool,
            pages[step_slot[k]],
            slot_length[k],
            score_scale,
        )
        context = result.astype(jnp.bfloat16).transpose(1, 0, 2).reshape(NEW, group * HEAD)
        partial = jnp.dot(context, full_out, preferred_element_type=jnp.float32).astype(
            jnp.bfloat16
        )
        pending = (k, partial)
    total = pending[1].astype(jnp.float32)
    for part in arrived_parts:
        total = total + part.astype(jnp.float32)
    return (total.astype(jnp.bfloat16), new_kv)


def solution(mesh):
    fine = jax.sharding.Mesh(mesh.devices.reshape(8, 2, 4, 2, 2), REQ_AXES + TP_AXES)
    in_specs = (
        P(REQ_AXES + TP_AXES, None),
        P(),
        P(REQ_AXES, TP_AXES),
        P(TP_AXES, REQ_AXES),
        P(),
        P(),
        P(REQ_AXES, None),
        P(REQ_AXES, None, TP_AXES),
    )
    out_specs = (P(REQ_AXES + TP_AXES, None), P(REQ_AXES, TP_AXES))
    return jax.shard_map(
        per_device, mesh=fine, in_specs=in_specs, out_specs=out_specs, check_vma=False
    )
```

```python
import math

import jax
import jax.numpy as jnp
from jax import lax
from jax.sharding import PartitionSpec as P

HEAD = 128
QH = 16
KVH = 4
PAGE = 128
NEW = 128


def rotate(values, position):
    half = values.shape[-1] // 2
    freqs = 500000.0 ** (-(jnp.arange(half, dtype=jnp.float32) * 2.0 / values.shape[-1]))
    angles = position.astype(jnp.float32)[:, None] * freqs[None, :]
    target = (angles.shape[0],) + (1,) * (values.ndim - 2) + (half,)
    cosine = jnp.cos(angles).reshape(target)
    sine = jnp.sin(angles).reshape(target)
    former = values[..., :half]
    latter = values[..., half:]
    return jnp.concatenate([former * cosine - latter * sine, latter * cosine + former * sine], -1)


def fresh_scores_of(query_matrix, recent_key_rows, score_scale):
    scores = (
        jnp.einsum("esv,qv->seq", query_matrix, recent_key_rows, preferred_element_type=jnp.float32)
        * score_scale
    )
    count_new = query_matrix.shape[0]
    causal = jnp.arange(count_new)[:, None] >= jnp.arange(count_new)[None, :]
    return jnp.where(causal, scores, -jnp.inf)


def value_weighted_rows(weights, values, form):
    return jnp.einsum(
        form, weights.astype(jnp.bfloat16), values, preferred_element_type=jnp.float32
    )


def padded_attention(
    query_matrix, recent_key_rows, recent_value_rows, pool, page_row, length, score_scale
):
    cache = pool[page_row].reshape(-1, 2 * HEAD)
    span = cache.shape[0]
    cached_scores = (
        jnp.einsum("ngd,kd->gnk", query_matrix, cache[:, :HEAD], preferred_element_type=jnp.float32)
        * score_scale
    )
    cached_scores = jnp.where(jnp.arange(span, dtype=jnp.int32) < length, cached_scores, -jnp.inf)
    recent_score_rows = fresh_scores_of(query_matrix, recent_key_rows, score_scale)
    row_max = jnp.maximum(cached_scores.max(-1), recent_score_rows.max(-1))[..., None]
    cached_exp = jnp.exp(cached_scores - row_max)
    recent_exponent = jnp.exp(recent_score_rows - row_max)
    total = cached_exp.sum(-1) + recent_exponent.sum(-1)
    summed_total = value_weighted_rows(cached_exp, cache[:, HEAD:], "gnk,kd->gnd")
    summed_total = summed_total + value_weighted_rows(
        recent_exponent, recent_value_rows, "vqa,as->vqs"
    )
    return summed_total / total[..., None]


REQ_AXES = ("z", "ylo", "x")
TP_AXES = ("yhi", "core")


def staged_gather(values, axes, axis):
    for name in reversed(axes):
        values = lax.all_gather(values, name, axis=axis, tiled=True)
    return values


def blocks_to_z_first(values, axis, sizes):
    shape = values.shape
    split = shape[:axis] + tuple(sizes) + (-1,) + shape[axis + 1:]
    order = tuple(range(axis)) + (axis + 2, axis + 1, axis) + tuple(range(axis + 3, len(split)))
    return values.reshape(split).transpose(order).reshape(shape)


def project_over_x(tokens, w_part):
    sizes = tuple(lax.axis_size(name) for name in REQ_AXES)
    n_x = sizes[-1]
    mine = lax.axis_index("x")
    held = lax.all_gather(lax.all_gather(w_part, "z", axis=0, tiled=True), "ylo", axis=0, tiled=True)
    ordered = blocks_to_z_first(tokens, 1, sizes)
    width = held.shape[0]
    total = None
    for k in range(n_x):
        block = held
        if k:
            block = lax.ppermute(held, "x", perm=[(s, (s - k) % n_x) for s in range(n_x)])
        features = lax.dynamic_slice_in_dim(ordered, ((mine + k) % n_x) * width, width, 1)
        term = jnp.dot(features, block, preferred_element_type=jnp.float32)
        total = term if total is None else total + term
    return total


def per_device(hidden, norm_gain, w_qkv, w_out, lengths, deal, pages, pool):
    states = hidden.astype(jnp.float32)
    mean_square = jnp.mean(states * states, axis=1, keepdims=True)
    normed = (states * lax.rsqrt(mean_square + 1e-05) * norm_gain.astype(jnp.float32)).astype(
        jnp.bfloat16
    )
    n_tp = lax.axis_size(TP_AXES)
    me = lax.axis_index(TP_AXES)
    arrived = [normed] + [
        lax.ppermute(normed, TP_AXES, perm=[(s, (s - k) % n_tp) for s in range(n_tp)])
        for k in range(1, n_tp)
    ]
    gathered = jnp.concatenate(arrived, 0)
    tok_rows = gathered.shape[0]
    cut = w_qkv.shape[1] // 2
    projected = jnp.concatenate(
        [
            jnp.dot(
                gathered,
                staged_gather(w_qkv[:, :cut], REQ_AXES, 0),
                preferred_element_type=jnp.float32,
            ),
            project_over_x(gathered, w_qkv[:, cut:]),
        ],
        1,
    ).astype(jnp.bfloat16)
    full_out = staged_gather(w_out, REQ_AXES, 1)
    group = QH // KVH
    heads_here = w_qkv.shape[1] // ((group + 2) * HEAD)
    assert heads_here == 1 and pool.shape[2] == 2 * HEAD
    slot_count = tok_rows // NEW
    step_slot = (me + jnp.arange(slot_count, dtype=jnp.int32)) % slot_count
    slot_ids = lax.axis_index(REQ_AXES) * slot_count + step_slot
    slot_length = lengths[deal[slot_ids]]
    position = jnp.repeat(slot_length, NEW) + jnp.tile(jnp.arange(NEW, dtype=jnp.int32), slot_count)
    projected = projected.reshape(tok_rows, group + 2, HEAD)
    queries = rotate(projected[:, :group].astype(jnp.float32), position).astype(jnp.bfloat16)
    keys_new = rotate(projected[:, group].astype(jnp.float32), position).astype(jnp.bfloat16)
    values_new = projected[:, group + 1]
    stepped_kv = jnp.concatenate([keys_new, values_new], 1)
    doubled = jnp.concatenate([stepped_kv, stepped_kv], 0)
    new_kv = lax.dynamic_slice_in_dim(doubled, ((slot_count - me) % slot_count) * NEW, tok_rows, 0)
    score_scale = 1.0 / math.sqrt(HEAD)

    total = None
    for k in range(slot_count):
        rows = slice(k * NEW, (k + 1) * NEW)
        result = padded_attention(
            queries[rows],
            keys_new[rows],
            values_new[rows],
            pool,
            pages[step_slot[k]],
            slot_length[k],
            score_scale,
        )
        context = result.astype(jnp.bfloat16).transpose(1, 0, 2).reshape(NEW, group * HEAD)
        partial = jnp.dot(context, full_out, preferred_element_type=jnp.float32).astype(
            jnp.bfloat16
        )
        if k:
            partial = lax.ppermute(partial, TP_AXES, perm=[(s, (s + k) % n_tp) for s in range(n_tp)])
        total = partial.astype(jnp.float32) if total is None else total + partial.astype(jnp.float32)
    return (total.astype(jnp.bfloat16), new_kv)


def solution(mesh):
    fine = jax.sharding.Mesh(mesh.devices.reshape(8, 2, 4, 2, 2), REQ_AXES + TP_AXES)
    in_specs = (
        P(REQ_AXES + TP_AXES, None),
        P(),
        P(REQ_AXES, TP_AXES),
        P(TP_AXES, REQ_AXES),
        P(),
        P(),
        P(REQ_AXES, None),
        P(REQ_AXES, None, TP_AXES),
    )
    out_specs = (P(REQ_AXES + TP_AXES, None), P(REQ_AXES, TP_AXES))
    return jax.shard_map(
        per_device, mesh=fine, in_specs=in_specs, out_specs=out_specs, check_vma=False
    )
```

```python
import math

import jax
import jax.numpy as jnp
from jax import lax
from jax.sharding import PartitionSpec as P

HEAD = 128
QH = 16
KVH = 4
PAGE = 128
NEW = 128


def rotate(values, position):
    half = values.shape[-1] // 2
    freqs = 500000.0 ** (-(jnp.arange(half, dtype=jnp.float32) * 2.0 / values.shape[-1]))
    angles = position.astype(jnp.float32)[:, None] * freqs[None, :]
    target = (angles.shape[0],) + (1,) * (values.ndim - 2) + (half,)
    cosine = jnp.cos(angles).reshape(target)
    sine = jnp.sin(angles).reshape(target)
    former = values[..., :half]
    latter = values[..., half:]
    return jnp.concatenate([former * cosine - latter * sine, latter * cosine + former * sine], -1)


def fresh_scores_of(query_matrix, recent_key_rows, score_scale):
    scores = (
        jnp.einsum("esv,qv->seq", query_matrix, recent_key_rows, preferred_element_type=jnp.float32)
        * score_scale
    )
    count_new = query_matrix.shape[0]
    causal = jnp.arange(count_new)[:, None] >= jnp.arange(count_new)[None, :]
    return jnp.where(causal, scores, -jnp.inf)


def value_weighted_rows(weights, values, form):
    return jnp.einsum(
        form, weights.astype(jnp.bfloat16), values, preferred_element_type=jnp.float32
    )


def padded_attention(
    query_matrix, recent_key_rows, recent_value_rows, pool, page_row, length, score_scale
):
    cache = pool[page_row].reshape(-1, 2 * HEAD)
    span = cache.shape[0]
    cached_scores = (
        jnp.einsum("ngd,kd->gnk", query_matrix, cache[:, :HEAD], preferred_element_type=jnp.float32)
        * score_scale
    )
    cached_scores = jnp.where(jnp.arange(span, dtype=jnp.int32) < length, cached_scores, -jnp.inf)
    recent_score_rows = fresh_scores_of(query_matrix, recent_key_rows, score_scale)
    row_max = jnp.maximum(cached_scores.max(-1), recent_score_rows.max(-1))[..., None]
    cached_exp = jnp.exp(cached_scores - row_max)
    recent_exponent = jnp.exp(recent_score_rows - row_max)
    total = cached_exp.sum(-1) + recent_exponent.sum(-1)
    summed_total = value_weighted_rows(cached_exp, cache[:, HEAD:], "gnk,kd->gnd")
    summed_total = summed_total + value_weighted_rows(
        recent_exponent, recent_value_rows, "vqa,as->vqs"
    )
    return summed_total / total[..., None]


REQ_AXES = ("z", "ylo", "x")
TP_AXES = ("yhi", "core")


def staged_gather(values, axes, axis):
    values = lax.all_gather(values, axes[1:], axis=axis, tiled=True)
    return lax.all_gather(values, axes[0], axis=axis, tiled=True)


def per_device(hidden, norm_gain, w_qkv, w_out, lengths, deal, pages, pool):
    states = hidden.astype(jnp.float32)
    mean_square = jnp.mean(states * states, axis=1, keepdims=True)
    normed = (states * lax.rsqrt(mean_square + 1e-05) * norm_gain.astype(jnp.float32)).astype(
        jnp.bfloat16
    )
    n_tp = lax.axis_size(TP_AXES)
    me = lax.axis_index(TP_AXES)
    arrived = [normed] + [
        lax.ppermute(normed, TP_AXES, perm=[(s, (s - k) % n_tp) for s in range(n_tp)])
        for k in range(1, n_tp)
    ]
    gathered = jnp.concatenate(arrived, 0)
    tok_rows = gathered.shape[0]
    projected = jnp.dot(
        gathered,
        staged_gather(w_qkv, REQ_AXES, 0),
        preferred_element_type=jnp.float32,
    ).astype(jnp.bfloat16)
    full_out = staged_gather(w_out, REQ_AXES, 1)
    group = QH // KVH
    heads_here = w_qkv.shape[1] // ((group + 2) * HEAD)
    assert heads_here == 1 and pool.shape[2] == 2 * HEAD
    slot_count = tok_rows // NEW
    step_slot = (me + jnp.arange(slot_count, dtype=jnp.int32)) % slot_count
    slot_ids = lax.axis_index(REQ_AXES) * slot_count + step_slot
    slot_length = lengths[deal[slot_ids]]
    position = jnp.repeat(slot_length, NEW) + jnp.tile(jnp.arange(NEW, dtype=jnp.int32), slot_count)
    projected = projected.reshape(tok_rows, group + 2, HEAD)
    queries = rotate(projected[:, :group].astype(jnp.float32), position).astype(jnp.bfloat16)
    keys_new = rotate(projected[:, group].astype(jnp.float32), position).astype(jnp.bfloat16)
    values_new = projected[:, group + 1]
    stepped_kv = jnp.concatenate([keys_new, values_new], 1)
    doubled = jnp.concatenate([stepped_kv, stepped_kv], 0)
    new_kv = lax.dynamic_slice_in_dim(doubled, ((slot_count - me) % slot_count) * NEW, tok_rows, 0)
    score_scale = 1.0 / math.sqrt(HEAD)

    total = None
    for k in range(slot_count):
        rows = slice(k * NEW, (k + 1) * NEW)
        result = padded_attention(
            queries[rows],
            keys_new[rows],
            values_new[rows],
            pool,
            pages[step_slot[k]],
            slot_length[k],
            score_scale,
        )
        context = result.astype(jnp.bfloat16).transpose(1, 0, 2).reshape(NEW, group * HEAD)
        partial = jnp.dot(context, full_out, preferred_element_type=jnp.float32).astype(
            jnp.bfloat16
        )
        if k:
            partial = lax.ppermute(partial, TP_AXES, perm=[(s, (s + k) % n_tp) for s in range(n_tp)])
        total = partial.astype(jnp.float32) if total is None else total + partial.astype(jnp.float32)
    return (total.astype(jnp.bfloat16), new_kv)


def solution(mesh):
    fine = jax.sharding.Mesh(mesh.devices.reshape(8, 2, 4, 2, 2), REQ_AXES + TP_AXES)
    in_specs = (
        P(REQ_AXES + TP_AXES, None),
        P(),
        P(REQ_AXES, TP_AXES),
        P(TP_AXES, REQ_AXES),
        P(),
        P(),
        P(REQ_AXES, None),
        P(REQ_AXES, None, TP_AXES),
    )
    out_specs = (P(REQ_AXES + TP_AXES, None), P(REQ_AXES, TP_AXES))
    return jax.shard_map(
        per_device, mesh=fine, in_specs=in_specs, out_specs=out_specs, check_vma=False
    )
```

```python
import math

import jax
import jax.numpy as jnp
from jax import lax
from jax.sharding import PartitionSpec as P

HEAD = 128
QH = 16
KVH = 4
PAGE = 128
NEW = 128


def rotate(values, position):
    half = values.shape[-1] // 2
    freqs = 500000.0 ** (-(jnp.arange(half, dtype=jnp.float32) * 2.0 / values.shape[-1]))
    angles = position.astype(jnp.float32)[:, None] * freqs[None, :]
    target = (angles.shape[0],) + (1,) * (values.ndim - 2) + (half,)
    cosine = jnp.cos(angles).reshape(target)
    sine = jnp.sin(angles).reshape(target)
    former = values[..., :half]
    latter = values[..., half:]
    return jnp.concatenate([former * cosine - latter * sine, latter * cosine + former * sine], -1)


def fresh_scores_of(query_matrix, recent_key_rows, score_scale):
    scores = (
        jnp.einsum("esv,qv->seq", query_matrix, recent_key_rows, preferred_element_type=jnp.float32)
        * score_scale
    )
    count_new = query_matrix.shape[0]
    causal = jnp.arange(count_new)[:, None] >= jnp.arange(count_new)[None, :]
    return jnp.where(causal, scores, -jnp.inf)


def value_weighted_rows(weights, values, form):
    return jnp.einsum(
        form, weights.astype(jnp.bfloat16), values, preferred_element_type=jnp.float32
    )


def padded_attention(
    query_matrix, recent_key_rows, recent_value_rows, pool, page_row, length, score_scale
):
    cache = pool[page_row].reshape(-1, 2 * HEAD)
    span = cache.shape[0]
    cached_scores = (
        jnp.einsum("ngd,kd->gnk", query_matrix, cache[:, :HEAD], preferred_element_type=jnp.float32)
        * score_scale
    )
    cached_scores = jnp.where(jnp.arange(span, dtype=jnp.int32) < length, cached_scores, -jnp.inf)
    recent_score_rows = fresh_scores_of(query_matrix, recent_key_rows, score_scale)
    row_max = jnp.maximum(cached_scores.max(-1), recent_score_rows.max(-1))[..., None]
    cached_exp = jnp.exp(cached_scores - row_max)
    recent_exponent = jnp.exp(recent_score_rows - row_max)
    total = cached_exp.sum(-1) + recent_exponent.sum(-1)
    summed_total = value_weighted_rows(cached_exp, cache[:, HEAD:], "gnk,kd->gnd")
    summed_total = summed_total + value_weighted_rows(
        recent_exponent, recent_value_rows, "vqa,as->vqs"
    )
    return summed_total / total[..., None]


REQ_AXES = ("z", "ylo", "x")
TP_AXES = ("yhi", "core")


def staged_gather(values, axes, axis):
    for name in reversed(axes):
        values = lax.all_gather(values, name, axis=axis, tiled=True)
    return values


def per_device(hidden, norm_gain, w_qkv, w_out, lengths, deal, pages, pool):
    states = hidden.astype(jnp.float32)
    mean_square = jnp.mean(states * states, axis=1, keepdims=True)
    normed = (states * lax.rsqrt(mean_square + 1e-05) * norm_gain.astype(jnp.float32)).astype(
        jnp.bfloat16
    )
    n_tp = lax.axis_size(TP_AXES)
    me = lax.axis_index(TP_AXES)
    arrived = [normed] + [
        lax.ppermute(normed, TP_AXES, perm=[(s, (s - k) % n_tp) for s in range(n_tp)])
        for k in range(1, n_tp)
    ]
    gathered = jnp.concatenate(arrived, 0)
    tok_rows = gathered.shape[0]
    projected = jnp.dot(
        gathered,
        staged_gather(w_qkv, REQ_AXES, 0),
        preferred_element_type=jnp.float32,
    ).astype(jnp.bfloat16)
    full_out = staged_gather(w_out, REQ_AXES, 1)
    group = QH // KVH
    heads_here = w_qkv.shape[1] // ((group + 2) * HEAD)
    assert heads_here == 1 and pool.shape[2] == 2 * HEAD
    slot_count = tok_rows // NEW
    step_slot = (me + jnp.arange(slot_count, dtype=jnp.int32)) % slot_count
    slot_ids = lax.axis_index(REQ_AXES) * slot_count + step_slot
    slot_length = lengths[deal[slot_ids]]
    position = jnp.repeat(slot_length, NEW) + jnp.tile(jnp.arange(NEW, dtype=jnp.int32), slot_count)
    projected = projected.reshape(tok_rows, group + 2, HEAD)
    queries = rotate(projected[:, :group].astype(jnp.float32), position).astype(jnp.bfloat16)
    keys_new = rotate(projected[:, group].astype(jnp.float32), position).astype(jnp.bfloat16)
    values_new = projected[:, group + 1]
    stepped_kv = jnp.concatenate([keys_new, values_new], 1)
    doubled = jnp.concatenate([stepped_kv, stepped_kv], 0)
    new_kv = lax.dynamic_slice_in_dim(doubled, ((slot_count - me) % slot_count) * NEW, tok_rows, 0)
    score_scale = 1.0 / math.sqrt(HEAD)

    contexts = []
    for k in range(slot_count):
        rows = slice(k * NEW, (k + 1) * NEW)
        result = padded_attention(
            queries[rows],
            keys_new[rows],
            values_new[rows],
            pool,
            pages[step_slot[k]],
            slot_length[k],
            score_scale,
        )
        contexts.append(result.astype(jnp.bfloat16).transpose(1, 0, 2).reshape(NEW, group * HEAD))
    partials = jnp.dot(
        jnp.concatenate(contexts, 0), full_out, preferred_element_type=jnp.float32
    ).astype(jnp.bfloat16)
    total = partials[:NEW].astype(jnp.float32)
    for k in range(1, slot_count):
        sent_to = [(s, (s + k) % n_tp) for s in range(n_tp)]
        arrived_part = lax.ppermute(partials[k * NEW:(k + 1) * NEW], TP_AXES, perm=sent_to)
        total = total + arrived_part.astype(jnp.float32)
    return (total.astype(jnp.bfloat16), new_kv)


def solution(mesh):
    fine = jax.sharding.Mesh(mesh.devices.reshape(8, 2, 4, 2, 2), REQ_AXES + TP_AXES)
    in_specs = (
        P(REQ_AXES + TP_AXES, None),
        P(),
        P(REQ_AXES, TP_AXES),
        P(TP_AXES, REQ_AXES),
        P(),
        P(),
        P(REQ_AXES, None),
        P(REQ_AXES, None, TP_AXES),
    )
    out_specs = (P(REQ_AXES + TP_AXES, None), P(REQ_AXES, TP_AXES))
    return jax.shard_map(
        per_device, mesh=fine, in_specs=in_specs, out_specs=out_specs, check_vma=False
    )
```

```python
import math

import jax
import jax.numpy as jnp
from jax import lax
from jax.sharding import PartitionSpec as P

HEAD = 128
QH = 16
KVH = 4
PAGE = 128
NEW = 128


def rotate(values, position):
    half = values.shape[-1] // 2
    freqs = 500000.0 ** (-(jnp.arange(half, dtype=jnp.float32) * 2.0 / values.shape[-1]))
    angles = position.astype(jnp.float32)[:, None] * freqs[None, :]
    target = (angles.shape[0],) + (1,) * (values.ndim - 2) + (half,)
    cosine = jnp.cos(angles).reshape(target)
    sine = jnp.sin(angles).reshape(target)
    former = values[..., :half]
    latter = values[..., half:]
    return jnp.concatenate([former * cosine - latter * sine, latter * cosine + former * sine], -1)


def fresh_scores_of(query_matrix, recent_key_rows, score_scale):
    scores = (
        jnp.einsum("esv,qv->seq", query_matrix, recent_key_rows, preferred_element_type=jnp.float32)
        * score_scale
    )
    count_new = query_matrix.shape[0]
    causal = jnp.arange(count_new)[:, None] >= jnp.arange(count_new)[None, :]
    return jnp.where(causal, scores, -jnp.inf)


def value_weighted_rows(weights, values, form):
    return jnp.einsum(
        form, weights.astype(jnp.bfloat16), values, preferred_element_type=jnp.float32
    )


def padded_attention(
    query_matrix, recent_key_rows, recent_value_rows, pool, page_row, length, score_scale
):
    cache = pool[page_row].reshape(-1, 2 * HEAD)
    span = cache.shape[0]
    cached_scores = (
        jnp.einsum("ngd,kd->gnk", query_matrix, cache[:, :HEAD], preferred_element_type=jnp.float32)
        * score_scale
    )
    cached_scores = jnp.where(jnp.arange(span, dtype=jnp.int32) < length, cached_scores, -jnp.inf)
    recent_score_rows = fresh_scores_of(query_matrix, recent_key_rows, score_scale)
    row_max = jnp.maximum(cached_scores.max(-1), recent_score_rows.max(-1))[..., None]
    cached_exp = jnp.exp(cached_scores - row_max)
    recent_exponent = jnp.exp(recent_score_rows - row_max)
    total = cached_exp.sum(-1) + recent_exponent.sum(-1)
    summed_total = value_weighted_rows(cached_exp, cache[:, HEAD:], "gnk,kd->gnd")
    summed_total = summed_total + value_weighted_rows(
        recent_exponent, recent_value_rows, "vqa,as->vqs"
    )
    return summed_total / total[..., None]


REQ_AXES = ("z", "ylo", "x")
TP_AXES = ("yhi", "core")


def staged_gather(values, axes, axis):
    for name in reversed(axes):
        values = lax.all_gather(values, name, axis=axis, tiled=True)
    return values


def per_device(hidden, norm_gain, w_qkv, w_out, lengths, deal, pages, pool):
    states = hidden.astype(jnp.float32)
    mean_square = jnp.mean(states * states, axis=1, keepdims=True)
    normed = (states * lax.rsqrt(mean_square + 1e-05) * norm_gain.astype(jnp.float32)).astype(
        jnp.bfloat16
    )
    n_tp = lax.axis_size(TP_AXES)
    me = lax.axis_index(TP_AXES)
    arrived = [normed] + [
        lax.ppermute(normed, TP_AXES, perm=[(s, (s - k) % n_tp) for s in range(n_tp)])
        for k in range(1, n_tp)
    ]
    gathered = jnp.concatenate(arrived, 0)
    tok_rows = gathered.shape[0]
    projected = jnp.dot(
        gathered,
        staged_gather(w_qkv, REQ_AXES, 0),
        preferred_element_type=jnp.float32,
    ).astype(jnp.bfloat16)
    full_out = staged_gather(w_out, REQ_AXES, 1)
    group = QH // KVH
    heads_here = w_qkv.shape[1] // ((group + 2) * HEAD)
    assert heads_here == 1 and pool.shape[2] == 2 * HEAD
    slot_count = tok_rows // NEW
    step_slot = (me + jnp.arange(slot_count, dtype=jnp.int32)) % slot_count
    slot_ids = lax.axis_index(REQ_AXES) * slot_count + step_slot
    slot_length = lengths[deal[slot_ids]]
    position = jnp.repeat(slot_length, NEW) + jnp.tile(jnp.arange(NEW, dtype=jnp.int32), slot_count)
    projected = projected.reshape(tok_rows, group + 2, HEAD)
    queries = rotate(projected[:, :group].astype(jnp.float32), position).astype(jnp.bfloat16)
    keys_new = rotate(projected[:, group].astype(jnp.float32), position).astype(jnp.bfloat16)
    values_new = projected[:, group + 1]
    stepped_kv = jnp.concatenate([keys_new, values_new], 1)
    doubled = jnp.concatenate([stepped_kv, stepped_kv], 0)
    new_kv = lax.dynamic_slice_in_dim(doubled, ((slot_count - me) % slot_count) * NEW, tok_rows, 0)
    score_scale = 1.0 / math.sqrt(HEAD)

    contexts = []
    for k in range(slot_count):
        rows = slice(k * NEW, (k + 1) * NEW)
        result = padded_attention(
            queries[rows],
            keys_new[rows],
            values_new[rows],
            pool,
            pages[step_slot[k]],
            slot_length[k],
            score_scale,
        )
        contexts.append(result.astype(jnp.bfloat16).transpose(1, 0, 2).reshape(NEW, group * HEAD))
    stepped = jnp.concatenate(contexts, 0)
    stepped = jnp.concatenate([stepped, stepped], 0)
    in_order = lax.dynamic_slice_in_dim(stepped, ((slot_count - me) % slot_count) * NEW, tok_rows, 0)
    partials = jnp.dot(in_order, full_out, preferred_element_type=jnp.float32).astype(jnp.bfloat16)
    n_hi = lax.axis_size("yhi")
    n_core = lax.axis_size("core")
    partials = partials.reshape(n_hi, n_core, NEW, partials.shape[-1])
    core = lax.axis_index("core")
    hi = lax.axis_index("yhi")
    kept = lax.dynamic_index_in_dim(partials, core, 1, keepdims=False)
    given = lax.dynamic_index_in_dim(partials, 1 - core, 1, keepdims=False)
    taken = lax.ppermute(given, "core", perm=[(0, 1), (1, 0)])
    pair_sum = kept.astype(jnp.float32) + taken.astype(jnp.float32)
    mine = lax.dynamic_index_in_dim(pair_sum, hi, 0, keepdims=False)
    theirs = lax.dynamic_index_in_dim(pair_sum, 1 - hi, 0, keepdims=False).astype(jnp.bfloat16)
    total = mine + lax.ppermute(theirs, "yhi", perm=[(0, 1), (1, 0)]).astype(jnp.float32)
    return (total.astype(jnp.bfloat16), new_kv)


def solution(mesh):
    fine = jax.sharding.Mesh(mesh.devices.reshape(8, 2, 4, 2, 2), REQ_AXES + TP_AXES)
    in_specs = (
        P(REQ_AXES + TP_AXES, None),
        P(),
        P(REQ_AXES, TP_AXES),
        P(TP_AXES, REQ_AXES),
        P(),
        P(),
        P(REQ_AXES, None),
        P(REQ_AXES, None, TP_AXES),
    )
    out_specs = (P(REQ_AXES + TP_AXES, None), P(REQ_AXES, TP_AXES))
    return jax.shard_map(
        per_device, mesh=fine, in_specs=in_specs, out_specs=out_specs, check_vma=False
    )
```

```python
import math

import jax
import jax.numpy as jnp
from jax import lax
from jax.sharding import PartitionSpec as P

HEAD = 128
QH = 16
KVH = 4
PAGE = 128
NEW = 128


def rotate(values, position):
    half = values.shape[-1] // 2
    freqs = 500000.0 ** (-(jnp.arange(half, dtype=jnp.float32) * 2.0 / values.shape[-1]))
    angles = position.astype(jnp.float32)[:, None] * freqs[None, :]
    target = (angles.shape[0],) + (1,) * (values.ndim - 2) + (half,)
    cosine = jnp.cos(angles).reshape(target)
    sine = jnp.sin(angles).reshape(target)
    former = values[..., :half]
    latter = values[..., half:]
    return jnp.concatenate([former * cosine - latter * sine, latter * cosine + former * sine], -1)


def fresh_scores_of(query_matrix, recent_key_rows, score_scale):
    scores = (
        jnp.einsum("esv,qv->seq", query_matrix, recent_key_rows, preferred_element_type=jnp.float32)
        * score_scale
    )
    count_new = query_matrix.shape[0]
    causal = jnp.arange(count_new)[:, None] >= jnp.arange(count_new)[None, :]
    return jnp.where(causal, scores, -jnp.inf)


def value_weighted_rows(weights, values, form):
    return jnp.einsum(
        form, weights.astype(jnp.bfloat16), values, preferred_element_type=jnp.float32
    )


def padded_attention(
    query_matrix, recent_key_rows, recent_value_rows, pool, page_row, length, score_scale
):
    cache = pool[page_row].reshape(-1, 2 * HEAD)
    span = cache.shape[0]
    cached_scores = (
        jnp.einsum("ngd,kd->gnk", query_matrix, cache[:, :HEAD], preferred_element_type=jnp.float32)
        * score_scale
    )
    cached_scores = jnp.where(jnp.arange(span, dtype=jnp.int32) < length, cached_scores, -jnp.inf)
    recent_score_rows = fresh_scores_of(query_matrix, recent_key_rows, score_scale)
    row_max = jnp.maximum(cached_scores.max(-1), recent_score_rows.max(-1))[..., None]
    cached_exp = jnp.exp(cached_scores - row_max)
    recent_exponent = jnp.exp(recent_score_rows - row_max)
    total = cached_exp.sum(-1) + recent_exponent.sum(-1)
    summed_total = value_weighted_rows(cached_exp, cache[:, HEAD:], "gnk,kd->gnd")
    summed_total = summed_total + value_weighted_rows(
        recent_exponent, recent_value_rows, "vqa,as->vqs"
    )
    return summed_total / total[..., None]


REQ_AXES = ("z", "ylo", "x")
TP_AXES = ("yhi", "core")


def staged_gather(values, axes, axis):
    for name in reversed(axes):
        values = lax.all_gather(values, name, axis=axis, tiled=True)
    return values


def z_first_gather(values, axis):
    for name in REQ_AXES:
        values = lax.all_gather(values, name, axis=axis, tiled=True)
    return values


def blocks_to_z_first(values, axis, sizes):
    shape = values.shape
    split = shape[:axis] + tuple(sizes) + (-1,) + shape[axis + 1:]
    order = tuple(range(axis)) + (axis + 2, axis + 1, axis) + tuple(range(axis + 3, len(split)))
    return values.reshape(split).transpose(order).reshape(shape)


def per_device(hidden, norm_gain, w_qkv, w_out, lengths, deal, pages, pool):
    states = hidden.astype(jnp.float32)
    mean_square = jnp.mean(states * states, axis=1, keepdims=True)
    normed = (states * lax.rsqrt(mean_square + 1e-05) * norm_gain.astype(jnp.float32)).astype(
        jnp.bfloat16
    )
    n_tp = lax.axis_size(TP_AXES)
    me = lax.axis_index(TP_AXES)
    arrived = [normed] + [
        lax.ppermute(normed, TP_AXES, perm=[(s, (s - k) % n_tp) for s in range(n_tp)])
        for k in range(1, n_tp)
    ]
    gathered = jnp.concatenate(arrived, 0)
    tok_rows = gathered.shape[0]
    req_sizes = tuple(lax.axis_size(name) for name in REQ_AXES)
    projected = jnp.dot(
        blocks_to_z_first(gathered, 1, req_sizes),
        z_first_gather(w_qkv, 0),
        preferred_element_type=jnp.float32,
    ).astype(jnp.bfloat16)
    full_out = staged_gather(w_out, REQ_AXES, 1)
    group = QH // KVH
    heads_here = w_qkv.shape[1] // ((group + 2) * HEAD)
    assert heads_here == 1 and pool.shape[2] == 2 * HEAD
    slot_count = tok_rows // NEW
    step_slot = (me + jnp.arange(slot_count, dtype=jnp.int32)) % slot_count
    slot_ids = lax.axis_index(REQ_AXES) * slot_count + step_slot
    slot_length = lengths[deal[slot_ids]]
    position = jnp.repeat(slot_length, NEW) + jnp.tile(jnp.arange(NEW, dtype=jnp.int32), slot_count)
    projected = projected.reshape(tok_rows, group + 2, HEAD)
    queries = rotate(projected[:, :group].astype(jnp.float32), position).astype(jnp.bfloat16)
    keys_new = rotate(projected[:, group].astype(jnp.float32), position).astype(jnp.bfloat16)
    values_new = projected[:, group + 1]
    stepped_kv = jnp.concatenate([keys_new, values_new], 1)
    doubled = jnp.concatenate([stepped_kv, stepped_kv], 0)
    new_kv = lax.dynamic_slice_in_dim(doubled, ((slot_count - me) % slot_count) * NEW, tok_rows, 0)
    score_scale = 1.0 / math.sqrt(HEAD)

    contexts = []
    for k in range(slot_count):
        rows = slice(k * NEW, (k + 1) * NEW)
        result = padded_attention(
            queries[rows],
            keys_new[rows],
            values_new[rows],
            pool,
            pages[step_slot[k]],
            slot_length[k],
            score_scale,
        )
        contexts.append(result.astype(jnp.bfloat16).transpose(1, 0, 2).reshape(NEW, group * HEAD))
    stepped = jnp.concatenate(contexts, 0)
    stepped = jnp.concatenate([stepped, stepped], 0)
    in_order = lax.dynamic_slice_in_dim(stepped, ((slot_count - me) % slot_count) * NEW, tok_rows, 0)
    partials = jnp.dot(in_order, full_out, preferred_element_type=jnp.float32).astype(jnp.bfloat16)
    n_hi = lax.axis_size("yhi")
    n_core = lax.axis_size("core")
    partials = partials.reshape(n_hi, n_core, NEW, partials.shape[-1])
    core = lax.axis_index("core")
    hi = lax.axis_index("yhi")
    kept = lax.dynamic_index_in_dim(partials, core, 1, keepdims=False)
    given = lax.dynamic_index_in_dim(partials, 1 - core, 1, keepdims=False)
    taken = lax.ppermute(given, "core", perm=[(0, 1), (1, 0)])
    pair_sum = kept.astype(jnp.float32) + taken.astype(jnp.float32)
    mine = lax.dynamic_index_in_dim(pair_sum, hi, 0, keepdims=False)
    theirs = lax.dynamic_index_in_dim(pair_sum, 1 - hi, 0, keepdims=False).astype(jnp.bfloat16)
    total = mine + lax.ppermute(theirs, "yhi", perm=[(0, 1), (1, 0)]).astype(jnp.float32)
    return (total.astype(jnp.bfloat16), new_kv)


def solution(mesh):
    fine = jax.sharding.Mesh(mesh.devices.reshape(8, 2, 4, 2, 2), REQ_AXES + TP_AXES)
    in_specs = (
        P(REQ_AXES + TP_AXES, None),
        P(),
        P(REQ_AXES, TP_AXES),
        P(TP_AXES, REQ_AXES),
        P(),
        P(),
        P(REQ_AXES, None),
        P(REQ_AXES, None, TP_AXES),
    )
    out_specs = (P(REQ_AXES + TP_AXES, None), P(REQ_AXES, TP_AXES))
    return jax.shard_map(
        per_device, mesh=fine, in_specs=in_specs, out_specs=out_specs, check_vma=False
    )
```

```python
import math

import jax
import jax.numpy as jnp
from jax import lax
from jax.sharding import PartitionSpec as P

HEAD = 128
QH = 16
KVH = 4
PAGE = 128
NEW = 128


def rotate(values, position):
    half = values.shape[-1] // 2
    freqs = 500000.0 ** (-(jnp.arange(half, dtype=jnp.float32) * 2.0 / values.shape[-1]))
    angles = position.astype(jnp.float32)[:, None] * freqs[None, :]
    target = (angles.shape[0],) + (1,) * (values.ndim - 2) + (half,)
    cosine = jnp.cos(angles).reshape(target)
    sine = jnp.sin(angles).reshape(target)
    former = values[..., :half]
    latter = values[..., half:]
    return jnp.concatenate([former * cosine - latter * sine, latter * cosine + former * sine], -1)


def fresh_scores_of(query_matrix, recent_key_rows, score_scale):
    scores = (
        jnp.einsum("esv,qv->seq", query_matrix, recent_key_rows, preferred_element_type=jnp.float32)
        * score_scale
    )
    count_new = query_matrix.shape[0]
    causal = jnp.arange(count_new)[:, None] >= jnp.arange(count_new)[None, :]
    return jnp.where(causal, scores, -jnp.inf)


def value_weighted_rows(weights, values, form):
    return jnp.einsum(
        form, weights.astype(jnp.bfloat16), values, preferred_element_type=jnp.float32
    )


def padded_attention(
    query_matrix, recent_key_rows, recent_value_rows, pool, page_row, length, score_scale
):
    cache = pool[page_row].reshape(-1, 2 * HEAD)
    span = cache.shape[0]
    cached_scores = (
        jnp.einsum("ngd,kd->gnk", query_matrix, cache[:, :HEAD], preferred_element_type=jnp.float32)
        * score_scale
    )
    cached_scores = jnp.where(jnp.arange(span, dtype=jnp.int32) < length, cached_scores, -jnp.inf)
    recent_score_rows = fresh_scores_of(query_matrix, recent_key_rows, score_scale)
    row_max = jnp.maximum(cached_scores.max(-1), recent_score_rows.max(-1))[..., None]
    cached_exp = jnp.exp(cached_scores - row_max)
    recent_exponent = jnp.exp(recent_score_rows - row_max)
    total = cached_exp.sum(-1) + recent_exponent.sum(-1)
    summed_total = value_weighted_rows(cached_exp, cache[:, HEAD:], "gnk,kd->gnd")
    summed_total = summed_total + value_weighted_rows(
        recent_exponent, recent_value_rows, "vqa,as->vqs"
    )
    return summed_total / total[..., None]


REQ_AXES = ("z", "ylo", "x")
TP_AXES = ("yhi", "core")


def staged_gather(values, axes, axis):
    for name in reversed(axes):
        values = lax.all_gather(values, name, axis=axis, tiled=True)
    return values


def per_device(hidden, norm_gain, w_qkv, w_out, lengths, deal, pages, pool):
    states = hidden.astype(jnp.float32)
    mean_square = jnp.mean(states * states, axis=1, keepdims=True)
    normed = (states * lax.rsqrt(mean_square + 1e-05) * norm_gain.astype(jnp.float32)).astype(
        jnp.bfloat16
    )
    n_tp = lax.axis_size(TP_AXES)
    me = lax.axis_index(TP_AXES)
    arrived = [normed] + [
        lax.ppermute(normed, TP_AXES, perm=[(s, s ^ k) for s in range(n_tp)])
        for k in range(1, n_tp)
    ]
    gathered = jnp.concatenate(arrived, 0)
    tok_rows = gathered.shape[0]
    projected = jnp.dot(
        gathered,
        staged_gather(w_qkv, REQ_AXES, 0),
        preferred_element_type=jnp.float32,
    ).astype(jnp.bfloat16)
    full_out = staged_gather(w_out, REQ_AXES, 1)
    group = QH // KVH
    heads_here = w_qkv.shape[1] // ((group + 2) * HEAD)
    assert heads_here == 1 and pool.shape[2] == 2 * HEAD
    slot_count = tok_rows // NEW
    step_slot = jnp.bitwise_xor(me, jnp.arange(slot_count, dtype=jnp.int32))
    slot_ids = lax.axis_index(REQ_AXES) * slot_count + step_slot
    slot_length = lengths[deal[slot_ids]]
    position = jnp.repeat(slot_length, NEW) + jnp.tile(jnp.arange(NEW, dtype=jnp.int32), slot_count)
    projected = projected.reshape(tok_rows, group + 2, HEAD)
    queries = rotate(projected[:, :group].astype(jnp.float32), position).astype(jnp.bfloat16)
    keys_new = rotate(projected[:, group].astype(jnp.float32), position).astype(jnp.bfloat16)
    values_new = projected[:, group + 1]
    stepped_kv = jnp.concatenate([keys_new, values_new], 1)
    new_kv = jnp.take(stepped_kv.reshape(slot_count, NEW, -1), step_slot, axis=0).reshape(tok_rows, -1)
    score_scale = 1.0 / math.sqrt(HEAD)

    def context_of(k):
        rows = slice(k * NEW, (k + 1) * NEW)
        result = padded_attention(
            queries[rows],
            keys_new[rows],
            values_new[rows],
            pool,
            pages[step_slot[k]],
            slot_length[k],
            score_scale,
        )
        return result.astype(jnp.bfloat16).transpose(1, 0, 2).reshape(NEW, group * HEAD)

    def pair_sum_of(first, second):
        both = jnp.concatenate([context_of(first), context_of(second)], 0)
        shares = jnp.dot(both, full_out, preferred_element_type=jnp.float32).astype(jnp.bfloat16)
        taken = lax.ppermute(shares[NEW:], "core", perm=[(0, 1), (1, 0)])
        return shares[:NEW].astype(jnp.float32) + taken.astype(jnp.float32)

    theirs = pair_sum_of(2, 3).astype(jnp.bfloat16)
    crossed = lax.ppermute(theirs, "yhi", perm=[(0, 1), (1, 0)])
    total = pair_sum_of(0, 1) + crossed.astype(jnp.float32)
    return (total.astype(jnp.bfloat16), new_kv)


def solution(mesh):
    fine = jax.sharding.Mesh(mesh.devices.reshape(8, 2, 4, 2, 2), REQ_AXES + TP_AXES)
    in_specs = (
        P(REQ_AXES + TP_AXES, None),
        P(),
        P(REQ_AXES, TP_AXES),
        P(TP_AXES, REQ_AXES),
        P(),
        P(),
        P(REQ_AXES, None),
        P(REQ_AXES, None, TP_AXES),
    )
    out_specs = (P(REQ_AXES + TP_AXES, None), P(REQ_AXES, TP_AXES))
    return jax.shard_map(
        per_device, mesh=fine, in_specs=in_specs, out_specs=out_specs, check_vma=False
    )
```

```python
import math

import jax
import jax.numpy as jnp
from jax import lax
from jax.sharding import PartitionSpec as P

HEAD = 128
QH = 16
KVH = 4
PAGE = 128
NEW = 128


def rotate(values, position):
    half = values.shape[-1] // 2
    freqs = 500000.0 ** (-(jnp.arange(half, dtype=jnp.float32) * 2.0 / values.shape[-1]))
    angles = position.astype(jnp.float32)[:, None] * freqs[None, :]
    target = (angles.shape[0],) + (1,) * (values.ndim - 2) + (half,)
    cosine = jnp.cos(angles).reshape(target)
    sine = jnp.sin(angles).reshape(target)
    former = values[..., :half]
    latter = values[..., half:]
    return jnp.concatenate([former * cosine - latter * sine, latter * cosine + former * sine], -1)


def fresh_scores_of(query_matrix, recent_key_rows, score_scale):
    scores = (
        jnp.einsum("esv,qv->seq", query_matrix, recent_key_rows, preferred_element_type=jnp.float32)
        * score_scale
    )
    count_new = query_matrix.shape[0]
    causal = jnp.arange(count_new)[:, None] >= jnp.arange(count_new)[None, :]
    return jnp.where(causal, scores, -jnp.inf)


def value_weighted_rows(weights, values, form):
    return jnp.einsum(
        form, weights.astype(jnp.bfloat16), values, preferred_element_type=jnp.float32
    )


def padded_attention(
    query_matrix, recent_key_rows, recent_value_rows, pool, page_row, length, score_scale
):
    cache = pool[page_row].reshape(-1, 2 * HEAD)
    span = cache.shape[0]
    cached_scores = (
        jnp.einsum("ngd,kd->gnk", query_matrix, cache[:, :HEAD], preferred_element_type=jnp.float32)
        * score_scale
    )
    cached_scores = jnp.where(jnp.arange(span, dtype=jnp.int32) < length, cached_scores, -jnp.inf)
    recent_score_rows = fresh_scores_of(query_matrix, recent_key_rows, score_scale)
    row_max = jnp.maximum(cached_scores.max(-1), recent_score_rows.max(-1))[..., None]
    cached_exp = jnp.exp(cached_scores - row_max)
    recent_exponent = jnp.exp(recent_score_rows - row_max)
    total = cached_exp.sum(-1) + recent_exponent.sum(-1)
    summed_total = value_weighted_rows(cached_exp, cache[:, HEAD:], "gnk,kd->gnd")
    summed_total = summed_total + value_weighted_rows(
        recent_exponent, recent_value_rows, "vqa,as->vqs"
    )
    return summed_total / total[..., None]


REQ_AXES = ("z", "ylo", "x")
TP_AXES = ("yhi", "core")


def staged_gather(values, axes, axis):
    for name in reversed(axes):
        values = lax.all_gather(values, name, axis=axis, tiled=True)
    return values


def per_device(hidden, norm_gain, w_qkv, w_out, lengths, deal, pages, pool):
    states = hidden.astype(jnp.float32)
    mean_square = jnp.mean(states * states, axis=1, keepdims=True)
    normed = (states * lax.rsqrt(mean_square + 1e-05) * norm_gain.astype(jnp.float32)).astype(
        jnp.bfloat16
    )
    n_tp = lax.axis_size(TP_AXES)
    me = lax.axis_index(TP_AXES)
    arrived = [normed] + [
        lax.ppermute(normed, TP_AXES, perm=[(s, s ^ k) for s in range(n_tp)])
        for k in range(1, n_tp)
    ]
    gathered = jnp.concatenate(arrived, 0)
    tok_rows = gathered.shape[0]
    projected = jnp.dot(
        gathered,
        staged_gather(w_qkv, REQ_AXES, 0),
        preferred_element_type=jnp.float32,
    ).astype(jnp.bfloat16)
    half = w_out.shape[1] // 2
    out_halves = [staged_gather(w_out[:, h * half:(h + 1) * half], REQ_AXES, 1) for h in range(2)]
    group = QH // KVH
    heads_here = w_qkv.shape[1] // ((group + 2) * HEAD)
    assert heads_here == 1 and pool.shape[2] == 2 * HEAD
    slot_count = tok_rows // NEW
    step_slot = jnp.bitwise_xor(me, jnp.arange(slot_count, dtype=jnp.int32))
    slot_ids = lax.axis_index(REQ_AXES) * slot_count + step_slot
    slot_length = lengths[deal[slot_ids]]
    position = jnp.repeat(slot_length, NEW) + jnp.tile(jnp.arange(NEW, dtype=jnp.int32), slot_count)
    projected = projected.reshape(tok_rows, group + 2, HEAD)
    queries = rotate(projected[:, :group].astype(jnp.float32), position).astype(jnp.bfloat16)
    keys_new = rotate(projected[:, group].astype(jnp.float32), position).astype(jnp.bfloat16)
    values_new = projected[:, group + 1]
    stepped_kv = jnp.concatenate([keys_new, values_new], 1)
    new_kv = jnp.take(stepped_kv.reshape(slot_count, NEW, -1), step_slot, axis=0).reshape(tok_rows, -1)
    score_scale = 1.0 / math.sqrt(HEAD)

    def context_of(k):
        rows = slice(k * NEW, (k + 1) * NEW)
        result = padded_attention(
            queries[rows],
            keys_new[rows],
            values_new[rows],
            pool,
            pages[step_slot[k]],
            slot_length[k],
            score_scale,
        )
        return result.astype(jnp.bfloat16).transpose(1, 0, 2).reshape(NEW, group * HEAD)

    def pair_sum_of(both, weights):
        shares = jnp.dot(both, weights, preferred_element_type=jnp.float32).astype(jnp.bfloat16)
        taken = lax.ppermute(shares[NEW:], "core", perm=[(0, 1), (1, 0)])
        return shares[:NEW].astype(jnp.float32) + taken.astype(jnp.float32)

    other_pair = jnp.concatenate([context_of(2), context_of(3)], 0)
    own_pair = jnp.concatenate([context_of(0), context_of(1)], 0)
    totals = []
    for weights in out_halves:
        theirs = pair_sum_of(other_pair, weights).astype(jnp.bfloat16)
        crossed = lax.ppermute(theirs, "yhi", perm=[(0, 1), (1, 0)])
        totals.append((pair_sum_of(own_pair, weights), crossed))
    total = jnp.stack([mine + crossed.astype(jnp.float32) for mine, crossed in totals], 2)
    n_req = out_halves[0].shape[1] // half
    total = total.reshape(NEW, n_req, half, 2).transpose(0, 1, 3, 2).reshape(NEW, -1)
    return (total.astype(jnp.bfloat16), new_kv)


def solution(mesh):
    fine = jax.sharding.Mesh(mesh.devices.reshape(8, 2, 4, 2, 2), REQ_AXES + TP_AXES)
    in_specs = (
        P(REQ_AXES + TP_AXES, None),
        P(),
        P(REQ_AXES, TP_AXES),
        P(TP_AXES, REQ_AXES),
        P(),
        P(),
        P(REQ_AXES, None),
        P(REQ_AXES, None, TP_AXES),
    )
    out_specs = (P(REQ_AXES + TP_AXES, None), P(REQ_AXES, TP_AXES))
    return jax.shard_map(
        per_device, mesh=fine, in_specs=in_specs, out_specs=out_specs, check_vma=False
    )
```
